256 devices in a mesh: space: 4 (over z_lo), rows: 8 (over y, core), cols: 8 (over z_hi, x).
Axes of the slice: x: 4, y: 4, z: 8 (z_hi: 2, z_lo: 4; z = z_hi * 4 + z_lo), core: 2. Of those that a mesh axis runs over, the one named last changes fastest.
Arguments:
- occupation: float32 [12288, 2048], P(('cols', 'rows'), 'space'), may hold values from -13.5 to 13.5, as said below
- propagator: float32 [12288, 12288], P('rows', 'cols'), may hold values from -0.5 to 1, as said below
- flags_first: int32 [12288, 2048], P(('cols', 'rows'), 'space'), may hold values from 0 to 2
- flags_second: int32 [12288, 2048], P(('rows', 'cols'), 'space'), may hold values from 0 to 2
- courant: float32 [12288], replicated, may hold values from -0.9 to 0.9
- weights: float32 [12288], replicated, may hold values from 0.5 to 6
Outputs:
- occupation_out: float32 [12288, 2048], P(('cols', 'rows'), 'space')
- temperature: float32 [2048], P('space')
The draws below stay inside these ranges and needn't reach their ends.
Inputs may be any that keep to these rules, and one draw needn't show every extreme that they name: occupation varies from mode to mode and cell to cell. propagator equals its transpose.
All inputs are finite; a program needn't handle non-finite values.
Results may differ from the reference program's by a relative error of at most 0.0003.
Values sent between devices are 32-bit elements; how exact they have to be, the bound alone decides.
No kernel may reach another device: no remote copies, remote signals or barrier semaphores. Data moves between devices by JAX's collectives and lax.ppermute only.
A program may use at most 64 MiB of HBM per device.

```python
import math
import jax
import jax.numpy as jnp
from jax import lax

M = 12288
NC = 2048


def draw_occupation(key, part):
    key_scale, key_offset, key_noise = jax.random.split(key, 3)
    scales = jnp.exp(jax.random.uniform(key_scale, (M, 1), jnp.float32, math.log(0.3), math.log(3.0)))
    offsets = jax.random.uniform(key_offset, (1, NC), jnp.float32, -1.5, 1.5)
    noise = jax.random.truncated_normal(key_noise, -4.0, 4.0, (M, NC), jnp.float32)
    return scales * noise + offsets


def draw_propagator(key, part):
    key_off, key_rate = jax.random.split(key, 2)
    raw = jax.random.truncated_normal(key_off, -4.0, 4.0, (M, M), jnp.float32)
    raw = raw * (0.3 / math.sqrt(M))
    symmetric = (raw + raw.T) * (1.0 / math.sqrt(2.0))
    rates = jnp.exp(jax.random.uniform(key_rate, (M,), jnp.float32, math.log(0.5), math.log(5.0)))
    positions = jnp.arange(M)
    return symmetric.at[positions, positions].set(1.0 - 0.15 * rates)


def draw_weights(key, part):
    rising = jnp.exp(math.log(3.0) * jnp.arange(M, dtype=jnp.float32) / M)
    spread = jnp.exp(jax.random.uniform(key, (M,), jnp.float32, math.log(0.5), math.log(2.0)))
    return rising * spread


def touch_ends(array, stream_key, low, top_value):
    place = [jax.random.randint(jax.random.fold_in(stream_key, axis), (), 0, length) for axis, length in enumerate(array.shape)]
    longest = array.shape.index(max(array.shape))
    next_to = place[:longest] + [(place[longest] + 1) % array.shape[longest]] + place[longest + 1:]
    return array.at[tuple(place)].set(low).at[tuple(next_to)].set(top_value)


def setup_inputs(seed: int = 0) -> dict:
    keys = jax.random.split(jax.random.key(seed), 7)
    return {
        "occupation": draw_occupation(jax.random.fold_in(keys[6], 71), 0),
        "propagator": draw_propagator(jax.random.fold_in(keys[6], 71), 0),
        "flags_first": touch_ends(jax.random.randint(keys[2], (M, NC), 0, 3), jax.random.fold_in(keys[2], 1), 0, 2).astype(jnp.int32),
        "flags_second": touch_ends(jax.random.randint(keys[3], (M, NC), 0, 3), jax.random.fold_in(keys[3], 1), 0, 2).astype(jnp.int32),
        "courant": jnp.clip(jax.random.uniform(keys[4], (M,), jnp.float32, -0.9, 0.9), -0.9, 0.9),
        "weights": draw_weights(jax.random.fold_in(keys[6], 71), 0),
    }


highest = lax.Precision.HIGHEST


def limited(left_diff, right_diff, selector):
    left_size = jnp.abs(left_diff)
    right_size = jnp.abs(right_diff)
    agreement = 0.5 * (jnp.sign(left_diff) + jnp.sign(right_diff))
    minmod_size = jnp.minimum(left_size, right_size)
    central_size = jnp.minimum(2.0 * minmod_size, 0.5 * jnp.abs(left_diff + right_diff))
    superbee_size = jnp.maximum(jnp.minimum(2.0 * left_size, right_size), jnp.minimum(left_size, 2.0 * right_size))
    chosen = jnp.where(selector == 0, minmod_size, jnp.where(selector == 1, central_size, superbee_size))
    return agreement * chosen


def advect(padded, selector, courant_col):
    differences = padded[:, 1:] - padded[:, :-1]
    slopes = limited(differences[:, :-1], differences[:, 1:], selector[:, 1:-1])
    centers = padded[:, 1:-1]
    forward = courant_col * (centers[:, :-1] + 0.5 * (1.0 - courant_col) * slopes[:, :-1])
    backward = courant_col * (centers[:, 1:] - 0.5 * (1.0 + courant_col) * slopes[:, 1:])
    fluxes = jnp.where(courant_col > 0.0, forward, backward)
    return padded[:, 2:-2] - (fluxes[:, 1:] - fluxes[:, :-1])


def split_step(field, selector, courant, weights, propagator):
    padded = jnp.pad(field, ((0, 0), (2, 2)))
    padded_flags = jnp.pad(selector, ((0, 0), (2, 2)))
    shifted = advect(padded, padded_flags, courant[:, None])
    heat = jnp.dot(weights, shifted, precision=highest) / jnp.sum(weights)
    deviation = shifted - weights[:, None] * heat[None, :]
    result = jnp.dot(propagator, deviation, precision=highest) + weights[:, None] * heat[None, :]
    return result, heat


def reference(occupation, propagator, flags_first, flags_second, courant, weights):
    middle, heat_first = split_step(occupation, flags_first, courant, weights, propagator)
    final, heat_second = split_step(middle, flags_second, courant, weights, propagator)
    return final, heat_second
```

```python
import jax
import jax.numpy as jnp
from jax import lax
from jax.sharding import Mesh
from jax.sharding import PartitionSpec as P

highest = lax.Precision.HIGHEST
high = lax.Precision.HIGH

ROWS = ("y", "core")
COLS = ("zh", "x")


def padded_2(block, sides, width):
    for axis, dim in sides:
        count = lax.axis_size(axis)
        forward = [(i, i + 1) for i in range(count - 1)]
        backward = [(target, source) for source, target in forward]
        low = lax.ppermute(
            lax.slice_in_dim(block, block.shape[dim] - width, None, axis=dim), axis, forward
        )
        high_part = lax.ppermute(lax.slice_in_dim(block, 0, width, axis=dim), axis, backward)
        block = jnp.concatenate([low, block, high_part], axis=dim)
    return block


def limited(left_diff, right_diff, selector):
    left_size = jnp.abs(left_diff)
    right_size = jnp.abs(right_diff)
    agreement = 0.5 * (jnp.sign(left_diff) + jnp.sign(right_diff))
    minmod_size = jnp.minimum(left_size, right_size)
    central_size = jnp.minimum(2.0 * minmod_size, 0.5 * jnp.abs(left_diff + right_diff))
    superbee_size = jnp.maximum(
        jnp.minimum(2.0 * left_size, right_size), jnp.minimum(left_size, 2.0 * right_size)
    )
    chosen = jnp.where(
        selector == 0.0, minmod_size, jnp.where(selector == 1.0, central_size, superbee_size)
    )
    return agreement * chosen


def advect(padded, selector, courant_col):
    differences = padded[:, 1:] - padded[:, :-1]
    slopes = limited(differences[:, :-1], differences[:, 1:], selector[:, 1:-1])
    centers = padded[:, 1:-1]
    forward = courant_col * (centers[:, :-1] + 0.5 * (1.0 - courant_col) * slopes[:, :-1])
    backward = courant_col * (centers[:, 1:] - 0.5 * (1.0 + courant_col) * slopes[:, 1:])
    fluxes = jnp.where(courant_col > 0.0, forward, backward)
    return padded[:, 2:-2] - (fluxes[:, 1:] - fluxes[:, :-1])


def advect_slab(field, selector, courant_part):
    stacked = jnp.stack([field, selector.astype(jnp.float32)])
    padded = padded_2(stacked, (("space", 2),), 2)
    return advect(padded[0], padded[1], courant_part[:, None])


def row_of(vector, blocks, width):
    n = vector.shape[0] // blocks
    return jnp.pad(vector.reshape(blocks, 1, n), ((0, 0), (0, 0), (0, width - n)))


def on_device(occupation, propagator, flags_first, flags_second, courant, weights):
    n_core = lax.axis_size("core")
    n_x = lax.axis_size("x")
    n_zh = lax.axis_size("zh")
    row_count = lax.axis_size("y") * n_core
    col_count = n_zh * n_x
    row_index = lax.axis_index("y") * n_core + lax.axis_index("core")
    col_index = lax.axis_index("zh") * n_x + lax.axis_index("x")
    local_modes, cells = occupation.shape
    tile = propagator.shape[0]
    weight_total = jnp.sum(weights)

    offset_first = (col_index * row_count + row_index) * local_modes
    weight_first = lax.dynamic_slice_in_dim(weights, offset_first, local_modes)
    courant_first = lax.dynamic_slice_in_dim(courant, offset_first, local_modes)
    shifted = advect_slab(occupation, flags_first, courant_first)
    gathered = lax.all_gather(shifted, ROWS, axis=0, tiled=True)
    weight_colblk = lax.dynamic_slice_in_dim(weights, col_index * tile, tile)
    heat_part = jnp.dot(weight_colblk, gathered, precision=highest)
    pw_part = jnp.dot(propagator, weight_colblk, precision=highest)
    product = jnp.dot(
        propagator, gathered, precision=high, preferred_element_type=jnp.float32
    ).reshape(col_count, local_modes, cells)
    extra = 8 - 2
    payload = jnp.concatenate(
        [
            product,
            jnp.broadcast_to(heat_part[None, None, :], (col_count, 1, cells)),
            row_of(pw_part, col_count, cells),
            jnp.zeros((col_count, extra, cells), jnp.float32),
        ],
        axis=1,
    )
    depth = payload.shape[1]
    payload = payload.reshape(n_zh, n_x, depth, cells).transpose(1, 0, 2, 3)
    payload = payload.reshape(n_x * n_zh * depth, cells)
    payload = lax.psum_scatter(payload, "x", scatter_dimension=0, tiled=True)
    summed = lax.psum_scatter(payload, "zh", scatter_dimension=0, tiled=True)
    heat = summed[local_modes] / weight_total
    pw_second = summed[local_modes + 1, :local_modes]
    offset_second = (row_index * col_count + col_index) * local_modes
    weight_second = lax.dynamic_slice_in_dim(weights, offset_second, local_modes)
    courant_second = lax.dynamic_slice_in_dim(courant, offset_second, local_modes)
    middle = summed[:local_modes] + (weight_second - pw_second)[:, None] * heat[None, :]

    shifted_second = advect_slab(middle, flags_second, courant_second)
    gathered_second = lax.all_gather(shifted_second, "zh", axis=0, tiled=False)
    gathered_second = lax.all_gather(gathered_second, "x", axis=0, tiled=False)
    gathered_second = gathered_second.transpose(1, 0, 2, 3).reshape(tile, cells)
    weight_rowblk = lax.dynamic_slice_in_dim(weights, row_index * tile, tile)
    heat_part_second = jnp.dot(weight_rowblk, gathered_second, precision=highest)
    pw_part_second = jnp.dot(weight_rowblk, propagator, precision=highest)
    product_second = lax.dot_general(
        propagator,
        gathered_second,
        (((0,), (0,)), ((), ())),
        precision=high,
        preferred_element_type=jnp.float32,
    ).reshape(row_count, local_modes, cells)
    slots = jnp.where(
        jnp.arange(row_count)[:, None] == row_index, heat_part_second[None, :], 0.0
    )
    extra_second = 16 - row_count - 1
    payload_second = jnp.concatenate(
        [
            product_second,
            jnp.broadcast_to(slots[None], (row_count, row_count, cells)),
            row_of(pw_part_second, row_count, cells),
            jnp.zeros((row_count, extra_second, cells), jnp.float32),
        ],
        axis=1,
    )
    final_sum = lax.psum_scatter(payload_second, ROWS, scatter_dimension=0, tiled=True)[0]
    heat_slots = final_sum[local_modes : local_modes + row_count]
    heat_second = heat_slots[0]
    for k in range(1, row_count):
        heat_second = heat_second + heat_slots[k]
    heat_second = heat_second / weight_total
    pw_first = final_sum[local_modes + row_count, :local_modes]
    final = final_sum[:local_modes] + (weight_first - pw_first)[:, None] * heat_second[None, :]
    return (final, heat_second)


def solution(mesh):
    n_space, n_rows, n_cols = (mesh.shape[a] for a in ("space", "rows", "cols"))
    split = Mesh(
        mesh.devices.reshape(n_space, n_rows // 2, 2, 2, n_cols // 2),
        ("space", "y", "core", "zh", "x"),
    )
    mode_cr = ("zh", "x", "y", "core")
    mode_rc = ("y", "core", "zh", "x")
    placed = (
        P(mode_cr, "space"),
        P(ROWS, COLS),
        P(mode_cr, "space"),
        P(mode_rc, "space"),
        P(),
        P(),
    )
    return jax.shard_map(
        on_device,
        mesh=split,
        in_specs=placed,
        out_specs=(P(mode_cr, "space"), P("space")),
        check_vma=False,
    )
```

```python
import jax
import jax.numpy as jnp
from jax import lax
from jax.sharding import Mesh
from jax.sharding import PartitionSpec as P

highest = lax.Precision.HIGHEST
high = lax.Precision.HIGH

ROWS = ("y", "core")
COLS = ("zh", "x")


def padded_2(block, sides, width):
    for axis, dim in sides:
        count = lax.axis_size(axis)
        forward = [(i, i + 1) for i in range(count - 1)]
        backward = [(target, source) for source, target in forward]
        low = lax.ppermute(
            lax.slice_in_dim(block, block.shape[dim] - width, None, axis=dim), axis, forward
        )
        high_part = lax.ppermute(lax.slice_in_dim(block, 0, width, axis=dim), axis, backward)
        block = jnp.concatenate([low, block, high_part], axis=dim)
    return block


def limited(left_diff, right_diff, selector):
    left_size = jnp.abs(left_diff)
    right_size = jnp.abs(right_diff)
    agreement = 0.5 * (jnp.sign(left_diff) + jnp.sign(right_diff))
    minmod_size = jnp.minimum(left_size, right_size)
    central_size = jnp.minimum(2.0 * minmod_size, 0.5 * jnp.abs(left_diff + right_diff))
    superbee_size = jnp.maximum(
        jnp.minimum(2.0 * left_size, right_size), jnp.minimum(left_size, 2.0 * right_size)
    )
    chosen = jnp.where(
        selector == 0.0, minmod_size, jnp.where(selector == 1.0, central_size, superbee_size)
    )
    return agreement * chosen


def advect(padded, selector, courant_col):
    differences = padded[:, 1:] - padded[:, :-1]
    slopes = limited(differences[:, :-1], differences[:, 1:], selector[:, 1:-1])
    centers = padded[:, 1:-1]
    forward = courant_col * (centers[:, :-1] + 0.5 * (1.0 - courant_col) * slopes[:, :-1])
    backward = courant_col * (centers[:, 1:] - 0.5 * (1.0 + courant_col) * slopes[:, 1:])
    fluxes = jnp.where(courant_col > 0.0, forward, backward)
    return padded[:, 2:-2] - (fluxes[:, 1:] - fluxes[:, :-1])


def advect_slab(field, selector, courant_part):
    stacked = jnp.stack([field, selector.astype(jnp.float32)])
    padded = padded_2(stacked, (("space", 2),), 2)
    return advect(padded[0], padded[1], courant_part[:, None])


def row_of(vector, blocks, width):
    n = vector.shape[0] // blocks
    return jnp.pad(vector.reshape(blocks, 1, n), ((0, 0), (0, 0), (0, width - n)))


def on_device(occupation, propagator, flags_first, flags_second, courant, weights):
    n_core = lax.axis_size("core")
    n_x = lax.axis_size("x")
    n_zh = lax.axis_size("zh")
    row_count = lax.axis_size("y") * n_core
    col_count = n_zh * n_x
    row_index = lax.axis_index("y") * n_core + lax.axis_index("core")
    col_index = lax.axis_index("zh") * n_x + lax.axis_index("x")
    local_modes, cells = occupation.shape
    tile = propagator.shape[0]
    weight_total = jnp.sum(weights)

    offset_first = (col_index * row_count + row_index) * local_modes
    weight_first = lax.dynamic_slice_in_dim(weights, offset_first, local_modes)
    courant_first = lax.dynamic_slice_in_dim(courant, offset_first, local_modes)
    shifted = advect_slab(occupation, flags_first, courant_first)
    gathered = lax.all_gather(shifted, ROWS, axis=0, tiled=True)
    weight_colblk = lax.dynamic_slice_in_dim(weights, col_index * tile, tile)
    heat_part = jnp.dot(weight_colblk, gathered, precision=highest)
    pw_part = jnp.dot(propagator, weight_colblk, precision=highest)
    product = jnp.dot(
        propagator, gathered, precision=high, preferred_element_type=jnp.float32
    ).reshape(col_count, local_modes, cells)
    extra = 8 - 2
    payload = jnp.concatenate(
        [
            product,
            jnp.broadcast_to(heat_part[None, None, :], (col_count, 1, cells)),
            row_of(pw_part, col_count, cells),
            jnp.zeros((col_count, extra, cells), jnp.float32),
        ],
        axis=1,
    )
    depth = payload.shape[1]
    payload = payload.reshape(n_zh, n_x, depth, cells).transpose(1, 0, 2, 3)
    payload = payload.reshape(n_x * n_zh * depth, cells)
    payload = lax.psum_scatter(payload, "x", scatter_dimension=0, tiled=True)
    payload = payload.reshape(n_zh, depth, cells)
    zh_index = lax.axis_index("zh")
    swap = [(0, 1), (1, 0)]
    mine = lax.dynamic_index_in_dim(payload, zh_index, 0, keepdims=False)
    theirs = lax.dynamic_index_in_dim(payload, 1 - zh_index, 0, keepdims=False)
    summed = mine + lax.ppermute(theirs, "zh", swap)
    heat = summed[local_modes] / weight_total
    pw_second = summed[local_modes + 1, :local_modes]
    offset_second = (row_index * col_count + col_index) * local_modes
    weight_second = lax.dynamic_slice_in_dim(weights, offset_second, local_modes)
    courant_second = lax.dynamic_slice_in_dim(courant, offset_second, local_modes)
    middle = summed[:local_modes] + (weight_second - pw_second)[:, None] * heat[None, :]

    shifted_second = advect_slab(middle, flags_second, courant_second)
    partner = lax.ppermute(shifted_second, "zh", swap)
    gathered_second = jnp.where(
        zh_index == 0,
        jnp.stack([shifted_second, partner]),
        jnp.stack([partner, shifted_second]),
    )
    gathered_second = lax.all_gather(gathered_second, "x", axis=0, tiled=False)
    gathered_second = gathered_second.transpose(1, 0, 2, 3).reshape(tile, cells)
    weight_rowblk = lax.dynamic_slice_in_dim(weights, row_index * tile, tile)
    heat_part_second = jnp.dot(weight_rowblk, gathered_second, precision=highest)
    pw_part_second = jnp.dot(weight_rowblk, propagator, precision=highest)
    product_second = lax.dot_general(
        propagator,
        gathered_second,
        (((0,), (0,)), ((), ())),
        precision=high,
        preferred_element_type=jnp.float32,
    ).reshape(row_count, local_modes, cells)
    slots = jnp.where(
        jnp.arange(row_count)[:, None] == row_index, heat_part_second[None, :], 0.0
    )
    extra_second = 16 - row_count - 1
    payload_second = jnp.concatenate(
        [
            product_second,
            jnp.broadcast_to(slots[None], (row_count, row_count, cells)),
            row_of(pw_part_second, row_count, cells),
            jnp.zeros((row_count, extra_second, cells), jnp.float32),
        ],
        axis=1,
    )
    final_sum = lax.psum_scatter(payload_second, ROWS, scatter_dimension=0, tiled=True)[0]
    heat_slots = final_sum[local_modes : local_modes + row_count]
    heat_second = heat_slots[0]
    for k in range(1, row_count):
        heat_second = heat_second + heat_slots[k]
    heat_second = heat_second / weight_total
    pw_first = final_sum[local_modes + row_count, :local_modes]
    final = final_sum[:local_modes] + (weight_first - pw_first)[:, None] * heat_second[None, :]
    return (final, heat_second)


def solution(mesh):
    n_space, n_rows, n_cols = (mesh.shape[a] for a in ("space", "rows", "cols"))
    split = Mesh(
        mesh.devices.reshape(n_space, n_rows // 2, 2, 2, n_cols // 2),
        ("space", "y", "core", "zh", "x"),
    )
    mode_cr = ("zh", "x", "y", "core")
    mode_rc = ("y", "core", "zh", "x")
    placed = (
        P(mode_cr, "space"),
        P(ROWS, COLS),
        P(mode_cr, "space"),
        P(mode_rc, "space"),
        P(),
        P(),
    )
    return jax.shard_map(
        on_device,
        mesh=split,
        in_specs=placed,
        out_specs=(P(mode_cr, "space"), P("space")),
        check_vma=False,
    )
```

```python
import jax
import jax.numpy as jnp
from jax import lax
from jax.sharding import Mesh
from jax.sharding import PartitionSpec as P

highest = lax.Precision.HIGHEST
high = lax.Precision.HIGH

ROWS = ("y", "core")
COLS = ("zh", "x")


def padded_2(block, sides, width):
    for axis, dim in sides:
        count = lax.axis_size(axis)
        forward = [(i, i + 1) for i in range(count - 1)]
        backward = [(target, source) for source, target in forward]
        low = lax.ppermute(
            lax.slice_in_dim(block, block.shape[dim] - width, None, axis=dim), axis, forward
        )
        high_part = lax.ppermute(lax.slice_in_dim(block, 0, width, axis=dim), axis, backward)
        block = jnp.concatenate([low, block, high_part], axis=dim)
    return block


def limited(left_diff, right_diff, selector):
    left_size = jnp.abs(left_diff)
    right_size = jnp.abs(right_diff)
    agreement = 0.5 * (jnp.sign(left_diff) + jnp.sign(right_diff))
    minmod_size = jnp.minimum(left_size, right_size)
    central_size = jnp.minimum(2.0 * minmod_size, 0.5 * jnp.abs(left_diff + right_diff))
    superbee_size = jnp.maximum(
        jnp.minimum(2.0 * left_size, right_size), jnp.minimum(left_size, 2.0 * right_size)
    )
    chosen = jnp.where(
        selector == 0.0, minmod_size, jnp.where(selector == 1.0, central_size, superbee_size)
    )
    return agreement * chosen


def advect(padded, selector, courant_col):
    differences = padded[:, 1:] - padded[:, :-1]
    slopes = limited(differences[:, :-1], differences[:, 1:], selector[:, 1:-1])
    centers = padded[:, 1:-1]
    forward = courant_col * (centers[:, :-1] + 0.5 * (1.0 - courant_col) * slopes[:, :-1])
    backward = courant_col * (centers[:, 1:] - 0.5 * (1.0 + courant_col) * slopes[:, 1:])
    fluxes = jnp.where(courant_col > 0.0, forward, backward)
    return padded[:, 2:-2] - (fluxes[:, 1:] - fluxes[:, :-1])


def advect_slab(field, selector, courant_part):
    stacked = jnp.stack([field, selector.astype(jnp.float32)])
    padded = padded_2(stacked, (("space", 2),), 2)
    return advect(padded[0], padded[1], courant_part[:, None])


def row_of(vector, blocks, width):
    n = vector.shape[0] // blocks
    return jnp.pad(vector.reshape(blocks, 1, n), ((0, 0), (0, 0), (0, width - n)))


def on_device(occupation, propagator, flags_first, flags_second, courant, weights):
    n_core = lax.axis_size("core")
    n_x = lax.axis_size("x")
    n_zh = lax.axis_size("zh")
    row_count = lax.axis_size("y") * n_core
    col_count = n_zh * n_x
    row_index = lax.axis_index("y") * n_core + lax.axis_index("core")
    col_index = lax.axis_index("zh") * n_x + lax.axis_index("x")
    local_modes, cells = occupation.shape
    tile = propagator.shape[0]
    weight_total = jnp.sum(weights)

    offset_first = (col_index * row_count + row_index) * local_modes
    weight_first = lax.dynamic_slice_in_dim(weights, offset_first, local_modes)
    courant_first = lax.dynamic_slice_in_dim(courant, offset_first, local_modes)
    shifted = advect_slab(occupation, flags_first, courant_first)
    gathered = lax.all_gather(shifted, ROWS, axis=0, tiled=True)
    weight_colblk = lax.dynamic_slice_in_dim(weights, col_index * tile, tile)
    heat_part = jnp.sum(weight_colblk[:, None] * gathered, axis=0)
    pw_part = jnp.dot(propagator, weight_colblk, precision=highest)
    chunks = 2
    chunk = local_modes // chunks
    blocks = propagator.reshape(col_count, chunks, chunk, tile)
    offset_second = (row_index * col_count + col_index) * local_modes
    weight_second = lax.dynamic_slice_in_dim(weights, offset_second, local_modes)
    courant_second = lax.dynamic_slice_in_dim(courant, offset_second, local_modes)
    weight_rowblk = lax.dynamic_slice_in_dim(weights, row_index * tile, tile)
    weight_rowparts = weight_rowblk.reshape(row_count, chunks, chunk)
    zh_index = lax.axis_index("zh")
    swap = [(0, 1), (1, 0)]
    heat = None
    pw_second = None
    product_second = None
    heat_part_second = None
    for k in range(chunks):
        rows_k = blocks[:, k].reshape(col_count * chunk, tile)
        product = jnp.dot(
            rows_k, gathered, precision=high, preferred_element_type=jnp.float32
        ).reshape(col_count, chunk, cells)
        parts = [product]
        if k == 0:
            parts += [
                jnp.broadcast_to(heat_part[None, None, :], (col_count, 1, cells)),
                row_of(pw_part, col_count, cells),
                jnp.zeros((col_count, 6, cells), jnp.float32),
            ]
        payload = jnp.concatenate(parts, axis=1) if len(parts) > 1 else product
        depth = payload.shape[1]
        payload = payload.reshape(n_zh, n_x, depth, cells).transpose(1, 0, 2, 3)
        payload = payload.reshape(n_x * n_zh * depth, cells)
        payload = lax.psum_scatter(payload, "x", scatter_dimension=0, tiled=True)
        payload = payload.reshape(n_zh, depth, cells)
        mine = lax.dynamic_index_in_dim(payload, zh_index, 0, keepdims=False)
        theirs = lax.dynamic_index_in_dim(payload, 1 - zh_index, 0, keepdims=False)
        summed = mine + lax.ppermute(theirs, "zh", swap)
        if k == 0:
            heat = summed[chunk] / weight_total
            pw_second = summed[chunk + 1, :local_modes]
        part = slice(k * chunk, (k + 1) * chunk)
        middle = summed[:chunk] + (weight_second[part] - pw_second[part])[:, None] * heat[None, :]

        shifted_second = advect_slab(middle, flags_second[part], courant_second[part])
        partner = lax.ppermute(shifted_second, "zh", swap)
        pair = jnp.where(
            zh_index == 0,
            jnp.stack([shifted_second, partner]),
            jnp.stack([partner, shifted_second]),
        )
        gathered_second = lax.all_gather(pair, "x", axis=0, tiled=False)
        gathered_second = gathered_second.transpose(1, 0, 2, 3).reshape(col_count * chunk, cells)
        weight_k = weight_rowparts[:, k].reshape(col_count * chunk)
        heat_k = jnp.sum(weight_k[:, None] * gathered_second, axis=0)
        product_k = lax.dot_general(
            rows_k,
            gathered_second,
            (((0,), (0,)), ((), ())),
            precision=high,
            preferred_element_type=jnp.float32,
        )
        if k == 0:
            heat_part_second, product_second = heat_k, product_k
        else:
            heat_part_second = heat_part_second + heat_k
            product_second = product_second + product_k
    pw_part_second = jnp.dot(weight_rowblk, propagator, precision=highest)
    product_second = product_second.reshape(row_count, local_modes, cells)
    slots = jnp.where(
        jnp.arange(row_count)[:, None] == row_index, heat_part_second[None, :], 0.0
    )
    extra_second = 16 - row_count - 1
    payload_second = jnp.concatenate(
        [
            product_second,
            jnp.broadcast_to(slots[None], (row_count, row_count, cells)),
            row_of(pw_part_second, row_count, cells),
            jnp.zeros((row_count, extra_second, cells), jnp.float32),
        ],
        axis=1,
    )
    final_sum = lax.psum_scatter(payload_second, ROWS, scatter_dimension=0, tiled=True)[0]
    heat_slots = final_sum[local_modes : local_modes + row_count]
    heat_second = heat_slots[0]
    for k in range(1, row_count):
        heat_second = heat_second + heat_slots[k]
    heat_second = heat_second / weight_total
    pw_first = final_sum[local_modes + row_count, :local_modes]
    final = final_sum[:local_modes] + (weight_first - pw_first)[:, None] * heat_second[None, :]
    return (final, heat_second)


def solution(mesh):
    n_space, n_rows, n_cols = (mesh.shape[a] for a in ("space", "rows", "cols"))
    split = Mesh(
        mesh.devices.reshape(n_space, n_rows // 2, 2, 2, n_cols // 2),
        ("space", "y", "core", "zh", "x"),
    )
    mode_cr = ("zh", "x", "y", "core")
    mode_rc = ("y", "core", "zh", "x")
    placed = (
        P(mode_cr, "space"),
        P(ROWS, COLS),
        P(mode_cr, "space"),
        P(mode_rc, "space"),
        P(),
        P(),
    )
    return jax.shard_map(
        on_device,
        mesh=split,
        in_specs=placed,
        out_specs=(P(mode_cr, "space"), P("space")),
        check_vma=False,
    )
```
